512 devices in a mesh: gx: 8 (over y), gy: 64 (over z, x, core).
Axes of the slice: x: 4, y: 8, z: 8, core: 2. Of those that a mesh axis runs over, the one named last changes fastest.
Arguments:
- source: float32 [512, 256, 128], P('gy', 'gx'), may hold values from -0.004 to 0.004
- mask: int32 [512, 256, 128], P('gy', 'gx'), may hold values from 0 to 2, as said below
- cond_x: float32 [512, 256, 128], P('gy', 'gx'), may hold values from 0.0012 to 0.06
- cond_y: float32 [512, 256, 128], P('gy', 'gx'), may hold values from 0.4 to 5
- cond_z: float32 [512, 256, 128], P('gy', 'gx'), may hold values from 0.0004 to 0.01
Outputs:
- solution: float32 [512, 256, 128], P('gy', 'gx')
The draws below stay inside these ranges and needn't reach their ends.
Inputs may be any that keep to these rules, and one draw needn't show every extreme that they name: `mask`: 0 marks a fluid cell, 1 a cut cell, 2 a solid cell.
All inputs are finite; a program needn't handle non-finite values.
Results may differ from the reference program's by a relative error of at most 0.00095.
Values sent between devices are 32-bit elements; how exact they have to be, the bound alone decides.
No kernel may reach another device: no remote copies, remote signals or barrier semaphores. Data moves between devices by JAX's collectives and lax.ppermute only.
A program may use at most 128 MiB of HBM per device.

```python
import math
import jax
import jax.numpy as jnp
from jax import lax

CZ = 128
LEVELS = 6
NX = 256
NY = 512


def draw_mask(key, part):
    keys = jax.random.split(key, 4)
    least = min(NY, NX, CZ)
    radius = jax.random.randint(keys[0], (), max(1, least // 8), max(2, least // 4 + 1))
    centre_y = jax.random.randint(keys[1], (), 0, NY)
    centre_x = jax.random.randint(keys[2], (), 0, NX)
    centre_z = jax.random.randint(keys[3], (), 0, CZ)
    along_y = (jnp.arange(NY, dtype=jnp.int32) - centre_y)[:, None, None]
    along_x = (jnp.arange(NX, dtype=jnp.int32) - centre_x)[None, :, None]
    along_z = (jnp.arange(CZ, dtype=jnp.int32) - centre_z)[None, None, :]
    distance = along_y * along_y + along_x * along_x + along_z * along_z
    solid = distance <= radius * radius
    shell = distance <= (radius + 2) * (radius + 2)
    return jnp.where(solid, 2, jnp.where(shell, 1, 0)).astype(jnp.int32)


def draw_source(key, part):
    keys = jax.random.split(key, 1)
    return jnp.clip(0.0008 * jax.random.normal(keys[0], (NY, NX, CZ), jnp.float32), -0.004, 0.004)


def log_between(key, lowest, highest):
    return jnp.exp(jax.random.uniform(key, (NY, NX, CZ), jnp.float32, math.log(lowest), math.log(highest)))


def coefficient(key, offset_tag, slab_depth, bounds):
    slab_start = jax.random.randint(jax.random.fold_in(key, 101), (), 0, NY - slab_depth + 1)
    row_index = jnp.arange(NY, dtype=jnp.int32)[:, None, None]
    inside = (row_index >= slab_start) & (row_index < slab_start + slab_depth)
    subkeys = jax.random.split(jax.random.fold_in(key, offset_tag), 2)
    outside_values = log_between(subkeys[0], bounds[0], bounds[1])
    inside_values = log_between(subkeys[1], bounds[2], bounds[3])
    return jnp.where(inside, inside_values, outside_values)


def draw_cond_x(key, part):
    return coefficient(key, 11, NY // 4, (0.003, 0.06, 0.003, 0.006))


def draw_cond_y(key, part):
    return coefficient(key, 12, NY // 4, (0.4, 2.5, 1.25, 2.5))


def draw_cond_z(key, part):
    return coefficient(key, 13, NY // 4, (0.001, 0.01, 0.001, 0.002))


def setup_inputs(seed: int = 0) -> dict:
    streams_of = jax.random.split(jax.random.key(seed), 6)
    return {
        "source": draw_source(jax.random.fold_in(streams_of[5], 71), 0),
        "mask": draw_mask(jax.random.fold_in(streams_of[5], 71), 0),
        "cond_x": draw_cond_x(jax.random.fold_in(streams_of[5], 71), 0),
        "cond_y": draw_cond_y(jax.random.fold_in(streams_of[5], 71), 0),
        "cond_z": draw_cond_z(jax.random.fold_in(streams_of[5], 71), 0),
    }


base_shift = 0.001
wall_term = 0.02


def ahead(field, axis):
    size = field.shape[axis]
    edge = jnp.zeros_like(lax.slice_in_dim(field, 0, 1, axis=axis))
    return jnp.concatenate([lax.slice_in_dim(field, 1, size, axis=axis), edge], axis=axis)


def behind(field, axis):
    size = field.shape[axis]
    edge = jnp.zeros_like(lax.slice_in_dim(field, 0, 1, axis=axis))
    return jnp.concatenate([edge, lax.slice_in_dim(field, 0, size - 1, axis=axis)], axis=axis)


def coarse_sum(field):
    depth, width, height = field.shape
    return field.reshape(depth // 2, 2, width // 2, 2, height // 2, 2).sum(axis=(1, 3, 5))


def coarse_face(face, axis, parity):
    picked = lax.slice_in_dim(face, parity, face.shape[axis], stride=2, axis=axis)
    return 0.125 * coarse_sum(jnp.repeat(picked, 2, axis=axis))


def prolong(field):
    return jnp.repeat(jnp.repeat(jnp.repeat(field, 2, axis=0), 2, axis=1), 2, axis=2)


def make_level(face_x, face_y, face_z, shift):
    level = {"face_x": face_x, "face_y": face_y, "face_z": face_z}
    level["low_x"] = behind(face_x, 1)
    level["low_y"] = behind(face_y, 0)
    level["low_z"] = behind(face_z, 2)
    level["diag"] = shift + face_x + level["low_x"] + face_y + level["low_y"] + face_z + level["low_z"]
    return level


def neighbour_terms(level, field):
    return (level["face_x"] * ahead(field, 1) + level["low_x"] * behind(field, 1)
            + level["face_z"] * ahead(field, 2) + level["low_z"] * behind(field, 2))


def line_solve(level, rhs):
    lower = -level["low_y"]
    upper = -level["face_y"]
    diag = level["diag"]

    def sweep(carry, row):
        ratio_prev, value_prev = carry
        below, middle, above, right = row
        pivot = middle - below * ratio_prev
        ratio = above / pivot
        value = (right - below * value_prev) / pivot
        return (ratio, value), (ratio, value)

    zero = jnp.zeros(rhs.shape[1:], jnp.float32)
    unused, (ratios, values) = lax.scan(sweep, (zero, zero), (lower, diag, upper, rhs))

    def back(after, row):
        ratio, value = row
        now = value - ratio * after
        return now, now

    unused, result = lax.scan(back, zero, (ratios, values), reverse=True)
    return result


def relax(level, field, rhs):
    if field is None:
        return line_solve(level, rhs)
    return line_solve(level, rhs + neighbour_terms(level, field))


def residual_of(level, field, rhs):
    applied = (level["diag"] * field - level["face_y"] * ahead(field, 0)
               - level["low_y"] * behind(field, 0) - neighbour_terms(level, field))
    return rhs - applied


def cycle(levels, depth, rhs):
    level = levels[depth]
    field = relax(level, None, rhs)
    if depth == len(levels) - 1:
        return relax(level, field, rhs)
    residual = residual_of(level, field, rhs)
    correction = cycle(levels, depth + 1, 0.25 * coarse_sum(residual))
    field = field + prolong(correction)
    return relax(level, field, rhs)


def reference(source, mask, cond_x, cond_y, cond_z):
    open_cells = (mask != 2).astype(jnp.float32)
    wall = (mask == 1).astype(jnp.float32)
    face_x = cond_x * open_cells * ahead(open_cells, 1)
    face_y = cond_y * open_cells * ahead(open_cells, 0)
    face_z = cond_z * open_cells * ahead(open_cells, 2)
    shift = base_shift + wall_term * wall
    levels = [make_level(face_x, face_y, face_z, shift)]
    for depth in range(1, LEVELS):
        face_x = coarse_face(face_x, 1, 1)
        face_y = coarse_face(face_y, 0, 1)
        face_z = coarse_face(face_z, 2, 1)
        shift = 0.25 * coarse_sum(shift)
        levels.append(make_level(face_x, face_y, face_z, shift))
    return cycle(levels, 0, source * open_cells)
```

```python
import jax
import jax.numpy as jnp
from jax import lax
from jax.sharding import Mesh
from jax.sharding import PartitionSpec as P

LEVELS = 6
GY = ("gy_0", "gy_1", "gy_2")


base_shift = 0.001
wall_term = 0.02


def in_blocks(x, dim, count):
    before, after = (x.shape[:dim], x.shape[dim + 1 :])
    return jnp.moveaxis(x.reshape(*before, count, -1, *after), dim, 0)


def in_order(parts, dim):
    parts = jnp.moveaxis(parts, 0, dim)
    shape = parts.shape
    return parts.reshape(*shape[:dim], shape[dim] * shape[dim + 1], *shape[dim + 2 :])


def turned_blocks(parts, axes, sequence):
    shape = [lax.axis_size(a) for a in axes]
    parts = parts.reshape(*shape, *parts.shape[1:])
    for k in sequence:
        parts = lax.all_to_all(parts, axes[k], split_axis=k, concat_axis=k, tiled=True)
    return parts.reshape(-1, *parts.shape[len(axes) :])


def exchange_by_chip(x, groups, sequence, split_dim, concat_dim):
    count = lax.axis_size(groups[0]) * lax.axis_size(groups[1])
    parts = in_blocks(x, split_dim, count)
    return in_order(turned_blocks(parts, groups, sequence), concat_dim)


def copy_for_each(x, axis):
    count = lax.axis_size(axis)
    return lax.all_to_all(jnp.broadcast_to(x[None], (count, *x.shape)), axis, 0, 0, tiled=True)


def gather_directly(x, axis, dim):
    parts = copy_for_each(x, axis)
    return in_order(parts, dim)


def padded(cells, sides, width):
    for axis, dim in sides:
        count = lax.axis_size(axis)
        ends = count - 1
        head = lax.slice_in_dim(cells, 0, width, axis=dim)
        tail = lax.slice_in_dim(cells, cells.shape[dim] - width, cells.shape[dim], axis=dim)
        cells = jnp.concatenate(
            [
                lax.ppermute(tail, axis, [(i, (i + 1) % count) for i in range(ends)]),
                cells,
                lax.ppermute(head, axis, [((i + 1) % count, i) for i in range(ends)]),
            ],
            axis=dim,
        )
    return cells


def with_halo(x, sides, width):
    edges = {}
    for axis, dim in sides:
        count, length = (lax.axis_size(axis), x.shape[dim])
        up = [(i, (i + 1) % count) for i in range(count - 1)]
        last = lax.slice_in_dim(x, length - width, length, axis=dim)
        leading = lax.slice_in_dim(x, 0, width, axis=dim)
        edges[dim] = (
            lax.ppermute(last, axis, up),
            lax.ppermute(leading, axis, [(b, a) for a, b in up]),
        )
    done = []
    for _, dim in sides:
        low, high = edges[dim]
        around = [(width, width) if d in done else (0, 0) for d in range(x.ndim)]
        x = jnp.concatenate([jnp.pad(low, around), x, jnp.pad(high, around)], axis=dim)
        done.append(dim)
    return x


def swapped(x, axis, stride):
    return lax.ppermute(x, axis, [(i, i ^ 1 << stride) for i in range(lax.axis_size(axis))])


def ahead(field, axis):
    size = field.shape[axis]
    edge = jnp.zeros_like(lax.slice_in_dim(field, 0, 1, axis=axis))
    return jnp.concatenate([lax.slice_in_dim(field, 1, size, axis=axis), edge], axis=axis)


def behind(field, axis):
    size = field.shape[axis]
    edge = jnp.zeros_like(lax.slice_in_dim(field, 0, 1, axis=axis))
    return jnp.concatenate([edge, lax.slice_in_dim(field, 0, size - 1, axis=axis)], axis=axis)


def coarse_sum(field):
    depth, width, height = field.shape
    return field.reshape(depth // 2, 2, width // 2, 2, height // 2, 2).sum(axis=(1, 3, 5))


def coarse_face(face, axis, parity):
    picked = lax.slice_in_dim(face, parity, face.shape[axis], stride=2, axis=axis)
    return 0.125 * coarse_sum(jnp.repeat(picked, 2, axis=axis))


def prolong(field):
    return jnp.repeat(jnp.repeat(jnp.repeat(field, 2, axis=0), 2, axis=1), 2, axis=2)


def upper_flag(bit):
    return lax.axis_index(GY) // 2**bit % 2


def line_factors(lower, diag, upper):
    denoms = [diag[0]]
    ratios = [upper[0] / diag[0]]
    for place in range(1, diag.shape[0]):
        pivot = diag[place] - lower[place] * ratios[place - 1]
        denoms.append(pivot)
        ratios.append(upper[place] / pivot)
    return (denoms, ratios)


def rows_solve(level, rhs):
    lower = level["lower"]
    denoms = level["denoms"]
    ratios = level["ratios"]
    count = rhs.shape[0]
    values = [rhs[0] / denoms[0]]
    for place in range(1, count):
        values.append((rhs[place] - lower[place] * values[place - 1]) / denoms[place])
    result = [values[count - 1]]
    for place in range(count - 2, -1, -1):
        result.append(values[place] - ratios[place] * result[-1])
    return jnp.stack(result[::-1])


def assemble(faces, group):
    face_x, low_x, face_y, low_y, face_z, shift = faces
    low_z = behind(face_z, 2)
    diag = shift + face_x + low_x + face_y + low_y + face_z + low_z
    level = {
        "face_x": face_x,
        "low_x": low_x,
        "face_y": face_y,
        "low_y": low_y,
        "face_z": face_z,
        "low_z": low_z,
        "diag": diag,
        "group": group,
    }
    level["lower"] = -low_y
    denoms, ratios = line_factors(-low_y, diag, -face_y)
    level["denoms"] = denoms
    level["ratios"] = ratios
    blank = jnp.zeros_like(diag)
    level["first_resp"] = rows_solve(level, blank.at[0].set(1.0))
    level["last_resp"] = rows_solve(level, blank.at[-1].set(1.0))
    level["alpha"] = low_y[0] * level["first_resp"][0]
    level["gamma"] = low_y[0] * level["first_resp"][-1]
    level["beta"] = face_y[-1] * level["last_resp"][0]
    level["delta"] = face_y[-1] * level["last_resp"][-1]
    return level


def forward_terms(alpha, beta, gamma, delta, head, tail):
    zeros = jnp.zeros_like(head)
    ones = jnp.ones_like(head)
    return (
        gamma * beta - alpha * delta,
        zeros,
        delta,
        gamma * head - alpha * tail,
        gamma,
        tail,
        -alpha,
        zeros,
        ones,
    )


def chain_forward(earlier, later):
    product = []
    for left_row in range(3):
        for column in range(3):
            product.append(
                later[3 * left_row] * earlier[column]
                + later[3 * left_row + 1] * earlier[3 + column]
                + later[3 * left_row + 2] * earlier[6 + column]
            )
    scale = product[8]
    return tuple((entry / scale for entry in product))


def chain_backward(earlier, later):
    return (later[0] + later[1] * earlier[0], later[1] * earlier[1])


def settle(alpha, beta, head, state):
    carry_q = state[2] / state[8]
    carry_p = state[5] / state[8]
    pivot = 1.0 - alpha * carry_q
    return ((head + alpha * carry_p) / pivot, beta / pivot, carry_q, carry_p)


def reduced_local(alpha, beta, gamma, delta, head, tail):
    zeros = jnp.zeros_like(head[:1])
    ones = jnp.ones_like(head[:1])
    identity = (ones, zeros, zeros, zeros, ones, zeros, zeros, zeros, ones)
    terms = forward_terms(alpha, beta, gamma, delta, head, tail)
    inclusive = lax.associative_scan(chain_forward, terms, axis=0)
    state = tuple(
        (jnp.concatenate([plain, entry[:-1]], axis=0) for plain, entry in zip(identity, inclusive))
    )
    start, slope, carry_q, carry_p = settle(alpha, beta, head, state)
    later = lax.associative_scan(chain_backward, (start, slope), reverse=True, axis=0)
    next_first = jnp.concatenate([later[0][1:], zeros], axis=0)
    first = start + slope * next_first
    return (carry_p + carry_q * first, next_first)


def pick_block(values, index, shape):
    return lax.dynamic_index_in_dim(values, index, 0, keepdims=False).reshape(shape)


def reduced_moved(level, head, tail):
    group = level["group"]
    shape = head.shape
    packed = jnp.stack(
        [level["alpha"], level["beta"], level["gamma"], level["delta"], head, tail]
    ).reshape(6, 1, -1)
    if group == 1:
        moved = exchange_by_chip(packed, (("gy_0", "gy_1"), "gy_2"), (1, 0), 2, 1)
        prev_last, next_first = reduced_local(
            moved[0], moved[1], moved[2], moved[3], moved[4], moved[5]
        )
        back = lax.all_to_all(
            jnp.stack([prev_last, next_first]), GY, split_axis=1, concat_axis=2, tiled=True
        )
        return (back[0, 0].reshape(shape), back[1, 0].reshape(shape))
    whole = gather_directly(packed, GY, 1)
    whole = whole.reshape(6, whole.shape[1] // group, group, -1)[:, :, 0]
    prev_last, next_first = reduced_local(
        whole[0], whole[1], whole[2], whole[3], whole[4], whole[5]
    )
    index = lax.axis_index(GY) // group
    return (pick_block(prev_last, index, shape), pick_block(next_first, index, shape))


def line_solve(level, rhs):
    local = rows_solve(level, rhs)
    prev_last, next_first = reduced_moved(level, local[0], local[-1])
    return (
        local
        + (level["low_y"][0] * prev_last)[None] * level["first_resp"]
        + (level["face_y"][-1] * next_first)[None] * level["last_resp"]
    )


def neighbour_terms(level, field):
    rim = padded(field, (("gx", 1),), 1)
    return (
        level["face_x"] * rim[:, 2:]
        + level["low_x"] * rim[:, :-2]
        + level["face_z"] * ahead(field, 2)
        + level["low_z"] * behind(field, 2)
    )


def relax(level, field, rhs):
    return line_solve(level, rhs + neighbour_terms(level, field))


WHOLE_FROM = 3


def gather_whole(block, depth):
    if depth == 2:
        axes, count = (("gx",) + GY, lax.axis_size(GY))
    else:
        axes, count = (("gx", "gy_0", "gy_1"), lax.axis_size(GY) // 2)
    parts = lax.all_gather(block, axes, axis=0)
    parts = parts.reshape(lax.axis_size("gx"), count, *block.shape)
    parts = jnp.moveaxis(parts, (0, 1), (3, 1))
    lead, rows, width, height = (block.shape[0], block.shape[1], block.shape[2], block.shape[3])
    return parts.reshape(lead, count * rows, lax.axis_size("gx") * width, height)


def whole_level(face_x, face_y, face_z, shift):
    low_x = behind(face_x, 1)
    low_y = behind(face_y, 0)
    low_z = behind(face_z, 2)
    diag = shift + face_x + low_x + face_y + low_y + face_z + low_z
    level = {
        "face_x": face_x,
        "low_x": low_x,
        "face_y": face_y,
        "low_y": low_y,
        "face_z": face_z,
        "low_z": low_z,
        "diag": diag,
        "lower": -low_y,
    }
    level["denoms"], level["ratios"] = line_factors(-low_y, diag, -face_y)
    return level


def whole_terms(level, field):
    return (
        level["face_x"] * ahead(field, 1)
        + level["low_x"] * behind(field, 1)
        + level["face_z"] * ahead(field, 2)
        + level["low_z"] * behind(field, 2)
    )


def whole_cycle(levels, depth, rhs):
    level = levels[depth]
    field = rows_solve(level, rhs)
    if depth == len(levels) - 1:
        return rows_solve(level, rhs + whole_terms(level, field))
    residual = whole_terms(level, field)
    correction = whole_cycle(levels, depth + 1, 0.25 * coarse_sum(residual))
    field = field + prolong(correction)
    return rows_solve(level, rhs + whole_terms(level, field))


def body(source, mask, cond_x, cond_y, cond_z):
    open_cells = (mask != 2).astype(jnp.float32)
    wall = (mask == 1).astype(jnp.float32)
    rim = with_halo(
        jnp.stack([cond_x * open_cells, cond_y * open_cells, open_cells]), (("gx", 2), (GY, 1)), 1
    )
    faces = (
        cond_x * open_cells * rim[2, 1:-1, 2:],
        rim[0, 1:-1, :-2] * open_cells,
        cond_y * open_cells * rim[2, 2:, 1:-1],
        rim[1, :-2, 1:-1] * open_cells,
        cond_z * open_cells * ahead(open_cells, 2),
        base_shift + wall_term * wall,
    )
    rhs = source * open_cells
    levels = []
    fields = []
    sources = []
    residual = rhs
    for depth in range(WHOLE_FROM):
        group = 1
        if depth > 0:
            face_x, low_x, face_y, low_y, face_z, shift = faces
            faces = (
                coarse_face(face_x, 1, 1),
                coarse_face(low_x, 1, 0),
                coarse_face(face_y, 0, 1),
                coarse_face(low_y, 0, 0),
                coarse_face(face_z, 2, 1),
                0.25 * coarse_sum(shift),
            )
            rhs = 0.25 * coarse_sum(residual)
            if depth >= 2:
                group = 2 ** (depth - 1)
                stacked = jnp.stack((rhs,) + faces)
                partner = swapped(stacked, GY, depth - 2)
                upper = upper_flag(depth - 2) == 1
                folded = jnp.concatenate(
                    [jnp.where(upper, partner, stacked), jnp.where(upper, stacked, partner)], axis=1
                )
                rhs = folded[0]
                faces = tuple((folded[place] for place in range(1, 7)))
        level = assemble(faces, group)
        field = line_solve(level, rhs)
        residual = neighbour_terms(level, field)
        levels.append(level)
        fields.append(field)
        sources.append(rhs)
    face_x, low_x, face_y, low_y, face_z, shift = faces
    coarse = jnp.stack(
        [
            coarse_face(face_x, 1, 1),
            coarse_face(face_y, 0, 1),
            coarse_face(face_z, 2, 1),
            0.25 * coarse_sum(shift),
        ]
    )
    whole = gather_whole(coarse, WHOLE_FROM)
    whole_rhs = gather_whole((0.25 * coarse_sum(residual))[None], WHOLE_FROM)[0]
    face_x, face_y, face_z, shift = (whole[0], whole[1], whole[2], whole[3])
    chain = [whole_level(face_x, face_y, face_z, shift)]
    for depth in range(WHOLE_FROM + 1, LEVELS):
        face_x = coarse_face(face_x, 1, 1)
        face_y = coarse_face(face_y, 0, 1)
        face_z = coarse_face(face_z, 2, 1)
        shift = 0.25 * coarse_sum(shift)
        chain.append(whole_level(face_x, face_y, face_z, shift))
    whole_correction = whole_cycle(chain, 0, whole_rhs)
    rows, width, height = coarse.shape[1:]
    spread = 2 ** max(WHOLE_FROM - 2, 0)
    correction = lax.dynamic_slice(
        whole_correction,
        (rows * (lax.axis_index(GY) // spread), width * lax.axis_index("gx"), 0),
        (rows, width, height),
    )
    for depth in range(WHOLE_FROM - 1, -1, -1):
        if depth < WHOLE_FROM - 1 and depth + 1 >= 2:
            half = correction.shape[0] // 2
            correction = lax.dynamic_slice_in_dim(correction, upper_flag(depth - 1) * half, half, 0)
        field = fields[depth] + prolong(correction)
        correction = relax(levels[depth], field, sources[depth])
    return correction


def solution(mesh):
    finer = Mesh(mesh.devices.reshape(mesh.shape["gx"], 8, 4, 2), ("gx", "gy_0", "gy_1", "gy_2"))
    return jax.shard_map(
        body,
        mesh=finer,
        in_specs=(
            P(GY, "gx", None),
            P(GY, "gx", None),
            P(GY, "gx", None),
            P(GY, "gx", None),
            P(GY, "gx", None),
        ),
        out_specs=P(GY, "gx", None),
        check_vma=False,
    )
```

```python
import jax
import jax.numpy as jnp
from jax import lax
from jax.sharding import Mesh
from jax.sharding import PartitionSpec as P

LEVELS = 6
GY = ("gy_0", "gy_1", "gy_2")


base_shift = 0.001
wall_term = 0.02


def in_blocks(x, dim, count):
    before, after = (x.shape[:dim], x.shape[dim + 1 :])
    return jnp.moveaxis(x.reshape(*before, count, -1, *after), dim, 0)


def in_order(parts, dim):
    parts = jnp.moveaxis(parts, 0, dim)
    shape = parts.shape
    return parts.reshape(*shape[:dim], shape[dim] * shape[dim + 1], *shape[dim + 2 :])


def turned_blocks(parts, axes, sequence):
    shape = [lax.axis_size(a) for a in axes]
    parts = parts.reshape(*shape, *parts.shape[1:])
    for k in sequence:
        parts = lax.all_to_all(parts, axes[k], split_axis=k, concat_axis=k, tiled=True)
    return parts.reshape(-1, *parts.shape[len(axes) :])


def exchange_by_chip(x, groups, sequence, split_dim, concat_dim):
    count = lax.axis_size(groups[0]) * lax.axis_size(groups[1])
    parts = in_blocks(x, split_dim, count)
    return in_order(turned_blocks(parts, groups, sequence), concat_dim)


def copy_for_each(x, axis):
    count = lax.axis_size(axis)
    return lax.all_to_all(jnp.broadcast_to(x[None], (count, *x.shape)), axis, 0, 0, tiled=True)


def gather_directly(x, axis, dim):
    parts = copy_for_each(x, axis)
    return in_order(parts, dim)


def padded(cells, sides, width):
    for axis, dim in sides:
        count = lax.axis_size(axis)
        ends = count - 1
        head = lax.slice_in_dim(cells, 0, width, axis=dim)
        tail = lax.slice_in_dim(cells, cells.shape[dim] - width, cells.shape[dim], axis=dim)
        cells = jnp.concatenate(
            [
                lax.ppermute(tail, axis, [(i, (i + 1) % count) for i in range(ends)]),
                cells,
                lax.ppermute(head, axis, [((i + 1) % count, i) for i in range(ends)]),
            ],
            axis=dim,
        )
    return cells


def with_halo(x, sides, width):
    edges = {}
    for axis, dim in sides:
        count, length = (lax.axis_size(axis), x.shape[dim])
        up = [(i, (i + 1) % count) for i in range(count - 1)]
        last = lax.slice_in_dim(x, length - width, length, axis=dim)
        leading = lax.slice_in_dim(x, 0, width, axis=dim)
        edges[dim] = (
            lax.ppermute(last, axis, up),
            lax.ppermute(leading, axis, [(b, a) for a, b in up]),
        )
    done = []
    for _, dim in sides:
        low, high = edges[dim]
        around = [(width, width) if d in done else (0, 0) for d in range(x.ndim)]
        x = jnp.concatenate([jnp.pad(low, around), x, jnp.pad(high, around)], axis=dim)
        done.append(dim)
    return x


def swapped(x, axis, stride):
    return lax.ppermute(x, axis, [(i, i ^ 1 << stride) for i in range(lax.axis_size(axis))])


def ahead(field, axis):
    size = field.shape[axis]
    edge = jnp.zeros_like(lax.slice_in_dim(field, 0, 1, axis=axis))
    return jnp.concatenate([lax.slice_in_dim(field, 1, size, axis=axis), edge], axis=axis)


def behind(field, axis):
    size = field.shape[axis]
    edge = jnp.zeros_like(lax.slice_in_dim(field, 0, 1, axis=axis))
    return jnp.concatenate([edge, lax.slice_in_dim(field, 0, size - 1, axis=axis)], axis=axis)


def pair_matrix(size, parity):
    rows = jnp.arange(size)[:, None]
    cols = jnp.arange(size // 2)[None, :]
    if parity is None:
        return (rows // 2 == cols).astype(jnp.float32)
    return (rows == 2 * cols + parity).astype(jnp.float32)


def coarse_pick(field, y_parity, x_parity, z_parity):
    depth, width, height = field.shape
    if y_parity is None:
        picked = field[0::2] + field[1::2]
    else:
        picked = field[y_parity::2]
    picked = jnp.dot(
        picked.reshape(-1, height), pair_matrix(height, z_parity), precision=lax.Precision.HIGHEST
    ).reshape(depth // 2, width, height // 2)
    return jnp.einsum(
        "xa,yxb->yab", pair_matrix(width, x_parity), picked, precision=lax.Precision.HIGHEST
    )


def coarse_sum(field):
    return coarse_pick(field, None, None, None)


def coarse_face(face, axis, parity):
    parities = [None, None, None]
    parities[axis] = parity
    return 0.25 * coarse_pick(face, *parities)


def prolong(field):
    depth, width, height = field.shape
    grown = jnp.repeat(field, 2, axis=0)
    grown = jnp.dot(
        grown.reshape(-1, height), pair_matrix(2 * height, None).T, precision=lax.Precision.HIGHEST
    ).reshape(2 * depth, width, 2 * height)
    return jnp.einsum(
        "xa,yab->yxb", pair_matrix(2 * width, None), grown, precision=lax.Precision.HIGHEST
    )


def upper_flag(bit):
    return lax.axis_index(GY) // 2**bit % 2


def line_factors(lower, diag, upper):
    denoms = [diag[0]]
    ratios = [upper[0] / diag[0]]
    for place in range(1, diag.shape[0]):
        pivot = diag[place] - lower[place] * ratios[place - 1]
        denoms.append(pivot)
        ratios.append(upper[place] / pivot)
    return (denoms, ratios)


def rows_solve(level, rhs):
    lower = level["lower"]
    denoms = level["denoms"]
    ratios = level["ratios"]
    count = rhs.shape[0]
    values = [rhs[0] / denoms[0]]
    for place in range(1, count):
        values.append((rhs[place] - lower[place] * values[place - 1]) / denoms[place])
    result = [values[count - 1]]
    for place in range(count - 2, -1, -1):
        result.append(values[place] - ratios[place] * result[-1])
    return jnp.stack(result[::-1])


def assemble(faces, group):
    face_x, low_x, face_y, low_y, face_z, shift = faces
    low_z = behind(face_z, 2)
    diag = shift + face_x + low_x + face_y + low_y + face_z + low_z
    level = {
        "face_x": face_x,
        "low_x": low_x,
        "face_y": face_y,
        "low_y": low_y,
        "face_z": face_z,
        "low_z": low_z,
        "diag": diag,
        "group": group,
    }
    level["lower"] = -low_y
    denoms, ratios = line_factors(-low_y, diag, -face_y)
    level["denoms"] = denoms
    level["ratios"] = ratios
    blank = jnp.zeros_like(diag)
    level["first_resp"] = rows_solve(level, blank.at[0].set(1.0))
    level["last_resp"] = rows_solve(level, blank.at[-1].set(1.0))
    level["alpha"] = low_y[0] * level["first_resp"][0]
    level["gamma"] = low_y[0] * level["first_resp"][-1]
    level["beta"] = face_y[-1] * level["last_resp"][0]
    level["delta"] = face_y[-1] * level["last_resp"][-1]
    return level


def forward_terms(alpha, beta, gamma, delta, head, tail):
    zeros = jnp.zeros_like(head)
    ones = jnp.ones_like(head)
    return (
        gamma * beta - alpha * delta,
        zeros,
        delta,
        gamma * head - alpha * tail,
        gamma,
        tail,
        -alpha,
        zeros,
        ones,
    )


def chain_forward(earlier, later):
    product = []
    for left_row in range(3):
        for column in range(3):
            product.append(
                later[3 * left_row] * earlier[column]
                + later[3 * left_row + 1] * earlier[3 + column]
                + later[3 * left_row + 2] * earlier[6 + column]
            )
    scale = product[8]
    return tuple((entry / scale for entry in product))


def chain_backward(earlier, later):
    return (later[0] + later[1] * earlier[0], later[1] * earlier[1])


def settle(alpha, beta, head, state):
    carry_q = state[2] / state[8]
    carry_p = state[5] / state[8]
    pivot = 1.0 - alpha * carry_q
    return ((head + alpha * carry_p) / pivot, beta / pivot, carry_q, carry_p)


def reduced_local(alpha, beta, gamma, delta, head, tail):
    zeros = jnp.zeros_like(head[:1])
    ones = jnp.ones_like(head[:1])
    identity = (ones, zeros, zeros, zeros, ones, zeros, zeros, zeros, ones)
    terms = forward_terms(alpha, beta, gamma, delta, head, tail)
    inclusive = lax.associative_scan(chain_forward, terms, axis=0)
    state = tuple(
        (jnp.concatenate([plain, entry[:-1]], axis=0) for plain, entry in zip(identity, inclusive))
    )
    start, slope, carry_q, carry_p = settle(alpha, beta, head, state)
    later = lax.associative_scan(chain_backward, (start, slope), reverse=True, axis=0)
    next_first = jnp.concatenate([later[0][1:], zeros], axis=0)
    first = start + slope * next_first
    return (carry_p + carry_q * first, next_first)


def pick_block(values, index, shape):
    return lax.dynamic_index_in_dim(values, index, 0, keepdims=False).reshape(shape)


def reduced_moved(level, head, tail):
    group = level["group"]
    shape = head.shape
    packed = jnp.stack(
        [level["alpha"], level["beta"], level["gamma"], level["delta"], head, tail]
    ).reshape(6, 1, -1)
    if group == 1:
        moved = exchange_by_chip(packed, (("gy_0", "gy_1"), "gy_2"), (1, 0), 2, 1)
        prev_last, next_first = reduced_local(
            moved[0], moved[1], moved[2], moved[3], moved[4], moved[5]
        )
        back = lax.all_to_all(
            jnp.stack([prev_last, next_first]), GY, split_axis=1, concat_axis=2, tiled=True
        )
        return (back[0, 0].reshape(shape), back[1, 0].reshape(shape))
    whole = gather_directly(packed, GY, 1)
    whole = whole.reshape(6, whole.shape[1] // group, group, -1)[:, :, 0]
    prev_last, next_first = reduced_local(
        whole[0], whole[1], whole[2], whole[3], whole[4], whole[5]
    )
    index = lax.axis_index(GY) // group
    return (pick_block(prev_last, index, shape), pick_block(next_first, index, shape))


def line_solve(level, rhs):
    local = rows_solve(level, rhs)
    prev_last, next_first = reduced_moved(level, local[0], local[-1])
    return (
        local
        + (level["low_y"][0] * prev_last)[None] * level["first_resp"]
        + (level["face_y"][-1] * next_first)[None] * level["last_resp"]
    )


def neighbour_terms(level, field):
    rim = padded(field, (("gx", 1),), 1)
    return (
        level["face_x"] * rim[:, 2:]
        + level["low_x"] * rim[:, :-2]
        + level["face_z"] * ahead(field, 2)
        + level["low_z"] * behind(field, 2)
    )


def relax(level, field, rhs):
    return line_solve(level, rhs + neighbour_terms(level, field))


def body(source, mask, cond_x, cond_y, cond_z):
    open_cells = (mask != 2).astype(jnp.float32)
    wall = (mask == 1).astype(jnp.float32)
    rim = with_halo(
        jnp.stack([cond_x * open_cells, cond_y * open_cells, open_cells]), (("gx", 2), (GY, 1)), 1
    )
    faces = (
        cond_x * open_cells * rim[2, 1:-1, 2:],
        rim[0, 1:-1, :-2] * open_cells,
        cond_y * open_cells * rim[2, 2:, 1:-1],
        rim[1, :-2, 1:-1] * open_cells,
        cond_z * open_cells * ahead(open_cells, 2),
        base_shift + wall_term * wall,
    )
    rhs = source * open_cells
    levels = []
    fields = []
    sources = []
    residual = rhs
    for depth in range(LEVELS):
        group = 1
        if depth > 0:
            face_x, low_x, face_y, low_y, face_z, shift = faces
            faces = (
                coarse_face(face_x, 1, 1),
                coarse_face(low_x, 1, 0),
                coarse_face(face_y, 0, 1),
                coarse_face(low_y, 0, 0),
                coarse_face(face_z, 2, 1),
                0.25 * coarse_sum(shift),
            )
            rhs = 0.25 * coarse_sum(residual)
            if depth >= 2:
                group = 2 ** (depth - 1)
                stacked = jnp.stack((rhs,) + faces)
                partner = swapped(stacked, GY, depth - 2)
                upper = upper_flag(depth - 2) == 1
                folded = jnp.concatenate(
                    [jnp.where(upper, partner, stacked), jnp.where(upper, stacked, partner)], axis=1
                )
                rhs = folded[0]
                faces = tuple((folded[place] for place in range(1, 7)))
        level = assemble(faces, group)
        field = line_solve(level, rhs)
        if depth == LEVELS - 1:
            field = relax(level, field, rhs)
        else:
            residual = neighbour_terms(level, field)
        levels.append(level)
        fields.append(field)
        sources.append(rhs)
    correction = fields[-1]
    for depth in range(LEVELS - 2, -1, -1):
        if depth + 1 >= 2:
            half = correction.shape[0] // 2
            correction = lax.dynamic_slice_in_dim(correction, upper_flag(depth - 1) * half, half, 0)
        field = fields[depth] + prolong(correction)
        correction = relax(levels[depth], field, sources[depth])
    return correction


def solution(mesh):
    finer = Mesh(mesh.devices.reshape(mesh.shape["gx"], 8, 4, 2), ("gx", "gy_0", "gy_1", "gy_2"))
    return jax.shard_map(
        body,
        mesh=finer,
        in_specs=(
            P(GY, "gx", None),
            P(GY, "gx", None),
            P(GY, "gx", None),
            P(GY, "gx", None),
            P(GY, "gx", None),
        ),
        out_specs=P(GY, "gx", None),
        check_vma=False,
    )
```

```python
import jax
import jax.numpy as jnp
from jax import lax
from jax.sharding import Mesh
from jax.sharding import PartitionSpec as P

LEVELS = 6
GY = ("gy_0", "gy_1", "gy_2")


base_shift = 0.001
wall_term = 0.02


def in_blocks(x, dim, count):
    before, after = (x.shape[:dim], x.shape[dim + 1 :])
    return jnp.moveaxis(x.reshape(*before, count, -1, *after), dim, 0)


def in_order(parts, dim):
    parts = jnp.moveaxis(parts, 0, dim)
    shape = parts.shape
    return parts.reshape(*shape[:dim], shape[dim] * shape[dim + 1], *shape[dim + 2 :])


def turned_blocks(parts, axes, sequence):
    shape = [lax.axis_size(a) for a in axes]
    parts = parts.reshape(*shape, *parts.shape[1:])
    for k in sequence:
        parts = lax.all_to_all(parts, axes[k], split_axis=k, concat_axis=k, tiled=True)
    return parts.reshape(-1, *parts.shape[len(axes) :])


def exchange_by_chip(x, groups, sequence, split_dim, concat_dim):
    count = lax.axis_size(groups[0]) * lax.axis_size(groups[1])
    parts = in_blocks(x, split_dim, count)
    return in_order(turned_blocks(parts, groups, sequence), concat_dim)


def copy_for_each(x, axis):
    count = lax.axis_size(axis)
    return lax.all_to_all(jnp.broadcast_to(x[None], (count, *x.shape)), axis, 0, 0, tiled=True)


def gather_directly(x, axis, dim):
    parts = copy_for_each(x, axis)
    return in_order(parts, dim)


def padded(cells, sides, width):
    for axis, dim in sides:
        count = lax.axis_size(axis)
        ends = count - 1
        head = lax.slice_in_dim(cells, 0, width, axis=dim)
        tail = lax.slice_in_dim(cells, cells.shape[dim] - width, cells.shape[dim], axis=dim)
        cells = jnp.concatenate(
            [
                lax.ppermute(tail, axis, [(i, (i + 1) % count) for i in range(ends)]),
                cells,
                lax.ppermute(head, axis, [((i + 1) % count, i) for i in range(ends)]),
            ],
            axis=dim,
        )
    return cells


def with_halo(x, sides, width):
    edges = {}
    for axis, dim in sides:
        count, length = (lax.axis_size(axis), x.shape[dim])
        up = [(i, (i + 1) % count) for i in range(count - 1)]
        last = lax.slice_in_dim(x, length - width, length, axis=dim)
        leading = lax.slice_in_dim(x, 0, width, axis=dim)
        edges[dim] = (
            lax.ppermute(last, axis, up),
            lax.ppermute(leading, axis, [(b, a) for a, b in up]),
        )
    done = []
    for _, dim in sides:
        low, high = edges[dim]
        around = [(width, width) if d in done else (0, 0) for d in range(x.ndim)]
        x = jnp.concatenate([jnp.pad(low, around), x, jnp.pad(high, around)], axis=dim)
        done.append(dim)
    return x


def swapped(x, axis, stride):
    return lax.ppermute(x, axis, [(i, i ^ 1 << stride) for i in range(lax.axis_size(axis))])


def ahead(field, axis):
    size = field.shape[axis]
    edge = jnp.zeros_like(lax.slice_in_dim(field, 0, 1, axis=axis))
    return jnp.concatenate([lax.slice_in_dim(field, 1, size, axis=axis), edge], axis=axis)


def behind(field, axis):
    size = field.shape[axis]
    edge = jnp.zeros_like(lax.slice_in_dim(field, 0, 1, axis=axis))
    return jnp.concatenate([edge, lax.slice_in_dim(field, 0, size - 1, axis=axis)], axis=axis)


def pair_matrix(size, parity):
    rows = jnp.arange(size)[:, None]
    cols = jnp.arange(size // 2)[None, :]
    if parity is None:
        return (rows // 2 == cols).astype(jnp.float32)
    return (rows == 2 * cols + parity).astype(jnp.float32)


def coarse_pick(field, y_parity, x_parity, z_parity):
    depth, width, height = field.shape
    if y_parity is None:
        picked = field[0::2] + field[1::2]
    else:
        picked = field[y_parity::2]
    picked = jnp.dot(
        picked.reshape(-1, height), pair_matrix(height, z_parity), precision=lax.Precision.HIGHEST
    ).reshape(depth // 2, width, height // 2)
    return jnp.einsum(
        "xa,yxb->yab", pair_matrix(width, x_parity), picked, precision=lax.Precision.HIGHEST
    )


def coarse_sum(field):
    return coarse_pick(field, None, None, None)


def coarse_face(face, axis, parity):
    parities = [None, None, None]
    parities[axis] = parity
    return 0.25 * coarse_pick(face, *parities)


def prolong(field):
    depth, width, height = field.shape
    grown = jnp.repeat(field, 2, axis=0)
    grown = jnp.dot(
        grown.reshape(-1, height), pair_matrix(2 * height, None).T, precision=lax.Precision.HIGHEST
    ).reshape(2 * depth, width, 2 * height)
    return jnp.einsum(
        "xa,yab->yxb", pair_matrix(2 * width, None), grown, precision=lax.Precision.HIGHEST
    )


def upper_flag(bit):
    return lax.axis_index(GY) // 2**bit % 2


def line_factors(lower, diag, upper):
    denoms = [diag[0]]
    ratios = [upper[0] / diag[0]]
    for place in range(1, diag.shape[0]):
        pivot = diag[place] - lower[place] * ratios[place - 1]
        denoms.append(pivot)
        ratios.append(upper[place] / pivot)
    return (denoms, ratios)


def rows_solve(level, rhs):
    lower = level["lower"]
    denoms = level["denoms"]
    ratios = level["ratios"]
    count = rhs.shape[0]
    values = [rhs[0] / denoms[0]]
    for place in range(1, count):
        values.append((rhs[place] - lower[place] * values[place - 1]) / denoms[place])
    result = [values[count - 1]]
    for place in range(count - 2, -1, -1):
        result.append(values[place] - ratios[place] * result[-1])
    return jnp.stack(result[::-1])


def assemble(faces, group):
    face_x, low_x, face_y, low_y, face_z, shift = faces
    low_z = behind(face_z, 2)
    diag = shift + face_x + low_x + face_y + low_y + face_z + low_z
    level = {
        "face_x": face_x,
        "low_x": low_x,
        "face_y": face_y,
        "low_y": low_y,
        "face_z": face_z,
        "low_z": low_z,
        "diag": diag,
        "group": group,
    }
    level["lower"] = -low_y
    denoms, ratios = line_factors(-low_y, diag, -face_y)
    level["denoms"] = denoms
    level["ratios"] = ratios
    blank = jnp.zeros_like(diag)
    level["first_resp"] = rows_solve(level, blank.at[0].set(1.0))
    level["last_resp"] = rows_solve(level, blank.at[-1].set(1.0))
    level["alpha"] = low_y[0] * level["first_resp"][0]
    level["gamma"] = low_y[0] * level["first_resp"][-1]
    level["beta"] = face_y[-1] * level["last_resp"][0]
    level["delta"] = face_y[-1] * level["last_resp"][-1]
    return level


def forward_terms(alpha, beta, gamma, delta, head, tail):
    zeros = jnp.zeros_like(head)
    ones = jnp.ones_like(head)
    return (
        gamma * beta - alpha * delta,
        zeros,
        delta,
        gamma * head - alpha * tail,
        gamma,
        tail,
        -alpha,
        zeros,
        ones,
    )


def chain_forward(earlier, later):
    product = []
    for left_row in range(3):
        for column in range(3):
            product.append(
                later[3 * left_row] * earlier[column]
                + later[3 * left_row + 1] * earlier[3 + column]
                + later[3 * left_row + 2] * earlier[6 + column]
            )
    scale = product[8]
    return tuple((entry / scale for entry in product))


def chain_backward(earlier, later):
    return (later[0] + later[1] * earlier[0], later[1] * earlier[1])


def settle(alpha, beta, head, state):
    carry_q = state[2] / state[8]
    carry_p = state[5] / state[8]
    pivot = 1.0 - alpha * carry_q
    return ((head + alpha * carry_p) / pivot, beta / pivot, carry_q, carry_p)


def reduced_local(alpha, beta, gamma, delta, head, tail):
    zeros = jnp.zeros_like(head[:1])
    ones = jnp.ones_like(head[:1])
    identity = (ones, zeros, zeros, zeros, ones, zeros, zeros, zeros, ones)
    terms = forward_terms(alpha, beta, gamma, delta, head, tail)
    inclusive = lax.associative_scan(chain_forward, terms, axis=0)
    state = tuple(
        (jnp.concatenate([plain, entry[:-1]], axis=0) for plain, entry in zip(identity, inclusive))
    )
    start, slope, carry_q, carry_p = settle(alpha, beta, head, state)
    later = lax.associative_scan(chain_backward, (start, slope), reverse=True, axis=0)
    next_first = jnp.concatenate([later[0][1:], zeros], axis=0)
    first = start + slope * next_first
    return (carry_p + carry_q * first, next_first)


def pick_block(values, index, shape):
    return lax.dynamic_index_in_dim(values, index, 0, keepdims=False).reshape(shape)


def reduced_moved(level, head, tail):
    group = level["group"]
    shape = head.shape
    packed = jnp.stack(
        [level["alpha"], level["beta"], level["gamma"], level["delta"], head, tail]
    ).reshape(6, 1, -1)
    if group == 1:
        parts = in_blocks(packed, 2, lax.axis_size(GY))
        moved = in_order(lax.all_to_all(parts, GY, 0, 0, tiled=True), 1)
        prev_last, next_first = reduced_local(
            moved[0], moved[1], moved[2], moved[3], moved[4], moved[5]
        )
        back = lax.all_to_all(
            jnp.stack([prev_last, next_first]), GY, split_axis=1, concat_axis=2, tiled=True
        )
        return (back[0, 0].reshape(shape), back[1, 0].reshape(shape))
    whole = gather_directly(packed, GY, 1)
    whole = whole.reshape(6, whole.shape[1] // group, group, -1)[:, :, 0]
    prev_last, next_first = reduced_local(
        whole[0], whole[1], whole[2], whole[3], whole[4], whole[5]
    )
    index = lax.axis_index(GY) // group
    return (pick_block(prev_last, index, shape), pick_block(next_first, index, shape))


def line_solve(level, rhs):
    local = rows_solve(level, rhs)
    prev_last, next_first = reduced_moved(level, local[0], local[-1])
    return (
        local
        + (level["low_y"][0] * prev_last)[None] * level["first_resp"]
        + (level["face_y"][-1] * next_first)[None] * level["last_resp"]
    )


def neighbour_terms(level, field):
    rim = padded(field, (("gx", 1),), 1)
    return (
        level["face_x"] * rim[:, 2:]
        + level["low_x"] * rim[:, :-2]
        + level["face_z"] * ahead(field, 2)
        + level["low_z"] * behind(field, 2)
    )


def relax(level, field, rhs):
    return line_solve(level, rhs + neighbour_terms(level, field))


def body(source, mask, cond_x, cond_y, cond_z):
    open_cells = (mask != 2).astype(jnp.float32)
    wall = (mask == 1).astype(jnp.float32)
    rim = with_halo(
        jnp.stack([cond_x * open_cells, cond_y * open_cells, open_cells]), (("gx", 2), (GY, 1)), 1
    )
    faces = (
        cond_x * open_cells * rim[2, 1:-1, 2:],
        rim[0, 1:-1, :-2] * open_cells,
        cond_y * open_cells * rim[2, 2:, 1:-1],
        rim[1, :-2, 1:-1] * open_cells,
        cond_z * open_cells * ahead(open_cells, 2),
        base_shift + wall_term * wall,
    )
    rhs = source * open_cells
    levels = []
    fields = []
    sources = []
    residual = rhs
    for depth in range(LEVELS):
        group = 1
        if depth > 0:
            face_x, low_x, face_y, low_y, face_z, shift = faces
            faces = (
                coarse_face(face_x, 1, 1),
                coarse_face(low_x, 1, 0),
                coarse_face(face_y, 0, 1),
                coarse_face(low_y, 0, 0),
                coarse_face(face_z, 2, 1),
                0.25 * coarse_sum(shift),
            )
            rhs = 0.25 * coarse_sum(residual)
            if depth >= 2:
                group = 2 ** (depth - 1)
                stacked = jnp.stack((rhs,) + faces)
                partner = swapped(stacked, GY, depth - 2)
                upper = upper_flag(depth - 2) == 1
                folded = jnp.concatenate(
                    [jnp.where(upper, partner, stacked), jnp.where(upper, stacked, partner)], axis=1
                )
                rhs = folded[0]
                faces = tuple((folded[place] for place in range(1, 7)))
        level = assemble(faces, group)
        field = line_solve(level, rhs)
        if depth == LEVELS - 1:
            field = relax(level, field, rhs)
        else:
            residual = neighbour_terms(level, field)
        levels.append(level)
        fields.append(field)
        sources.append(rhs)
    correction = fields[-1]
    for depth in range(LEVELS - 2, -1, -1):
        if depth + 1 >= 2:
            half = correction.shape[0] // 2
            correction = lax.dynamic_slice_in_dim(correction, upper_flag(depth - 1) * half, half, 0)
        field = fields[depth] + prolong(correction)
        correction = relax(levels[depth], field, sources[depth])
    return correction


def solution(mesh):
    finer = Mesh(mesh.devices.reshape(mesh.shape["gx"], 8, 4, 2), ("gx", "gy_0", "gy_1", "gy_2"))
    return jax.shard_map(
        body,
        mesh=finer,
        in_specs=(
            P(GY, "gx", None),
            P(GY, "gx", None),
            P(GY, "gx", None),
            P(GY, "gx", None),
            P(GY, "gx", None),
        ),
        out_specs=P(GY, "gx", None),
        check_vma=False,
    )
```

```python
import jax
import jax.numpy as jnp
from jax import lax
from jax.sharding import Mesh
from jax.sharding import PartitionSpec as P

LEVELS = 6
GY = ("gy_0", "gy_1", "gy_2")


base_shift = 0.001
wall_term = 0.02


def in_blocks(x, dim, count):
    before, after = (x.shape[:dim], x.shape[dim + 1 :])
    return jnp.moveaxis(x.reshape(*before, count, -1, *after), dim, 0)


def in_order(parts, dim):
    parts = jnp.moveaxis(parts, 0, dim)
    shape = parts.shape
    return parts.reshape(*shape[:dim], shape[dim] * shape[dim + 1], *shape[dim + 2 :])


def turned_blocks(parts, axes, sequence):
    shape = [lax.axis_size(a) for a in axes]
    parts = parts.reshape(*shape, *parts.shape[1:])
    for k in sequence:
        parts = lax.all_to_all(parts, axes[k], split_axis=k, concat_axis=k, tiled=True)
    return parts.reshape(-1, *parts.shape[len(axes) :])


def exchange_by_chip(x, groups, sequence, split_dim, concat_dim):
    count = lax.axis_size(groups[0]) * lax.axis_size(groups[1])
    parts = in_blocks(x, split_dim, count)
    return in_order(turned_blocks(parts, groups, sequence), concat_dim)


def copy_for_each(x, axis):
    count = lax.axis_size(axis)
    return lax.all_to_all(jnp.broadcast_to(x[None], (count, *x.shape)), axis, 0, 0, tiled=True)


def gather_directly(x, axis, dim):
    parts = copy_for_each(x, axis)
    return in_order(parts, dim)


def padded(cells, sides, width):
    for axis, dim in sides:
        count = lax.axis_size(axis)
        ends = count - 1
        head = lax.slice_in_dim(cells, 0, width, axis=dim)
        tail = lax.slice_in_dim(cells, cells.shape[dim] - width, cells.shape[dim], axis=dim)
        cells = jnp.concatenate(
            [
                lax.ppermute(tail, axis, [(i, (i + 1) % count) for i in range(ends)]),
                cells,
                lax.ppermute(head, axis, [((i + 1) % count, i) for i in range(ends)]),
            ],
            axis=dim,
        )
    return cells


def with_halo(x, sides, width):
    edges = {}
    for axis, dim in sides:
        count, length = (lax.axis_size(axis), x.shape[dim])
        up = [(i, (i + 1) % count) for i in range(count - 1)]
        last = lax.slice_in_dim(x, length - width, length, axis=dim)
        leading = lax.slice_in_dim(x, 0, width, axis=dim)
        edges[dim] = (
            lax.ppermute(last, axis, up),
            lax.ppermute(leading, axis, [(b, a) for a, b in up]),
        )
    done = []
    for _, dim in sides:
        low, high = edges[dim]
        around = [(width, width) if d in done else (0, 0) for d in range(x.ndim)]
        x = jnp.concatenate([jnp.pad(low, around), x, jnp.pad(high, around)], axis=dim)
        done.append(dim)
    return x


def swapped(x, axis, stride):
    return lax.ppermute(x, axis, [(i, i ^ 1 << stride) for i in range(lax.axis_size(axis))])


def ahead(field, axis):
    size = field.shape[axis]
    edge = jnp.zeros_like(lax.slice_in_dim(field, 0, 1, axis=axis))
    return jnp.concatenate([lax.slice_in_dim(field, 1, size, axis=axis), edge], axis=axis)


def behind(field, axis):
    size = field.shape[axis]
    edge = jnp.zeros_like(lax.slice_in_dim(field, 0, 1, axis=axis))
    return jnp.concatenate([edge, lax.slice_in_dim(field, 0, size - 1, axis=axis)], axis=axis)


def pair_matrix(size, parity):
    rows = jnp.arange(size)[:, None]
    cols = jnp.arange(size // 2)[None, :]
    if parity is None:
        return (rows // 2 == cols).astype(jnp.float32)
    return (rows == 2 * cols + parity).astype(jnp.float32)


def coarse_pick(field, y_parity, x_parity, z_parity):
    depth, width, height = field.shape
    if y_parity is None:
        picked = field[0::2] + field[1::2]
    else:
        picked = field[y_parity::2]
    picked = jnp.dot(
        picked.reshape(-1, height), pair_matrix(height, z_parity), precision=lax.Precision.HIGHEST
    ).reshape(depth // 2, width, height // 2)
    return jnp.einsum(
        "xa,yxb->yab", pair_matrix(width, x_parity), picked, precision=lax.Precision.HIGHEST
    )


def coarse_sum(field):
    return coarse_pick(field, None, None, None)


def coarse_face(face, axis, parity):
    parities = [None, None, None]
    parities[axis] = parity
    return 0.25 * coarse_pick(face, *parities)


def prolong(field):
    depth, width, height = field.shape
    grown = jnp.repeat(field, 2, axis=0)
    grown = jnp.dot(
        grown.reshape(-1, height), pair_matrix(2 * height, None).T, precision=lax.Precision.HIGHEST
    ).reshape(2 * depth, width, 2 * height)
    return jnp.einsum(
        "xa,yab->yxb", pair_matrix(2 * width, None), grown, precision=lax.Precision.HIGHEST
    )


def upper_flag(bit):
    return lax.axis_index(GY) // 2**bit % 2


def line_factors(lower, diag, upper):
    denoms = [diag[0]]
    ratios = [upper[0] / diag[0]]
    for place in range(1, diag.shape[0]):
        pivot = diag[place] - lower[place] * ratios[place - 1]
        denoms.append(pivot)
        ratios.append(upper[place] / pivot)
    return (denoms, ratios)


def rows_solve(level, rhs):
    lower = level["lower"]
    denoms = level["denoms"]
    ratios = level["ratios"]
    count = rhs.shape[0]
    values = [rhs[0] / denoms[0]]
    for place in range(1, count):
        values.append((rhs[place] - lower[place] * values[place - 1]) / denoms[place])
    result = [values[count - 1]]
    for place in range(count - 2, -1, -1):
        result.append(values[place] - ratios[place] * result[-1])
    return jnp.stack(result[::-1])


def assemble(faces, group):
    face_x, low_x, face_y, low_y, face_z, shift = faces
    low_z = behind(face_z, 2)
    diag = shift + face_x + low_x + face_y + low_y + face_z + low_z
    level = {
        "face_x": face_x,
        "low_x": low_x,
        "face_y": face_y,
        "low_y": low_y,
        "face_z": face_z,
        "low_z": low_z,
        "diag": diag,
        "group": group,
    }
    level["lower"] = -low_y
    denoms, ratios = line_factors(-low_y, diag, -face_y)
    level["denoms"] = denoms
    level["ratios"] = ratios
    blank = jnp.zeros_like(diag)
    level["first_resp"] = rows_solve(level, blank.at[0].set(1.0))
    level["last_resp"] = rows_solve(level, blank.at[-1].set(1.0))
    level["alpha"] = low_y[0] * level["first_resp"][0]
    level["gamma"] = low_y[0] * level["first_resp"][-1]
    level["beta"] = face_y[-1] * level["last_resp"][0]
    level["delta"] = face_y[-1] * level["last_resp"][-1]
    return level


def forward_terms(alpha, beta, gamma, delta, head, tail):
    zeros = jnp.zeros_like(head)
    ones = jnp.ones_like(head)
    return (
        gamma * beta - alpha * delta,
        zeros,
        delta,
        gamma * head - alpha * tail,
        gamma,
        tail,
        -alpha,
        zeros,
        ones,
    )


def chain_forward(earlier, later):
    product = []
    for left_row in range(3):
        for column in range(3):
            product.append(
                later[3 * left_row] * earlier[column]
                + later[3 * left_row + 1] * earlier[3 + column]
                + later[3 * left_row + 2] * earlier[6 + column]
            )
    scale = product[8]
    return tuple((entry / scale for entry in product))


def chain_backward(earlier, later):
    return (later[0] + later[1] * earlier[0], later[1] * earlier[1])


def settle(alpha, beta, head, state):
    carry_q = state[2] / state[8]
    carry_p = state[5] / state[8]
    pivot = 1.0 - alpha * carry_q
    return ((head + alpha * carry_p) / pivot, beta / pivot, carry_q, carry_p)


def reduced_local(alpha, beta, gamma, delta, head, tail):
    zeros = jnp.zeros_like(head[:1])
    ones = jnp.ones_like(head[:1])
    identity = (ones, zeros, zeros, zeros, ones, zeros, zeros, zeros, ones)
    terms = forward_terms(alpha, beta, gamma, delta, head, tail)
    inclusive = lax.associative_scan(chain_forward, terms, axis=0)
    state = tuple(
        (jnp.concatenate([plain, entry[:-1]], axis=0) for plain, entry in zip(identity, inclusive))
    )
    start, slope, carry_q, carry_p = settle(alpha, beta, head, state)
    later = lax.associative_scan(chain_backward, (start, slope), reverse=True, axis=0)
    next_first = jnp.concatenate([later[0][1:], zeros], axis=0)
    first = start + slope * next_first
    return (carry_p + carry_q * first, next_first)


def pick_block(values, index, shape):
    return lax.dynamic_index_in_dim(values, index, 0, keepdims=False).reshape(shape)


def reduced_moved(level, head, tail):
    group = level["group"]
    shape = head.shape
    packed = jnp.stack(
        [level["alpha"], level["beta"], level["gamma"], level["delta"], head, tail]
    ).reshape(6, -1)
    if group == 1:
        parts = in_blocks(packed, 1, lax.axis_size(GY))
        moved = jnp.moveaxis(turned_blocks(parts, (("gy_0", "gy_1"), "gy_2"), (1, 0)), 0, 1)
        prev_last, next_first = reduced_local(
            moved[0], moved[1], moved[2], moved[3], moved[4], moved[5]
        )
        back = lax.all_to_all(
            jnp.stack([prev_last, next_first]), GY, split_axis=1, concat_axis=2, tiled=True
        )
        return (back[0, 0].reshape(shape), back[1, 0].reshape(shape))
    whole = jnp.moveaxis(copy_for_each(packed, GY), 0, 1)
    whole = whole.reshape(6, whole.shape[1] // group, group, -1)[:, :, 0]
    prev_last, next_first = reduced_local(
        whole[0], whole[1], whole[2], whole[3], whole[4], whole[5]
    )
    index = lax.axis_index(GY) // group
    return (pick_block(prev_last, index, shape), pick_block(next_first, index, shape))


def line_solve(level, rhs):
    local = rows_solve(level, rhs)
    prev_last, next_first = reduced_moved(level, local[0], local[-1])
    return (
        local
        + (level["low_y"][0] * prev_last)[None] * level["first_resp"]
        + (level["face_y"][-1] * next_first)[None] * level["last_resp"]
    )


def neighbour_terms(level, field):
    rim = padded(field, (("gx", 1),), 1)
    return (
        level["face_x"] * rim[:, 2:]
        + level["low_x"] * rim[:, :-2]
        + level["face_z"] * ahead(field, 2)
        + level["low_z"] * behind(field, 2)
    )


def relax(level, field, rhs):
    return line_solve(level, rhs + neighbour_terms(level, field))


def body(source, mask, cond_x, cond_y, cond_z):
    open_cells = (mask != 2).astype(jnp.float32)
    wall = (mask == 1).astype(jnp.float32)
    rim = with_halo(
        jnp.stack([cond_x * open_cells, cond_y * open_cells, open_cells]), (("gx", 2), (GY, 1)), 1
    )
    faces = (
        cond_x * open_cells * rim[2, 1:-1, 2:],
        rim[0, 1:-1, :-2] * open_cells,
        cond_y * open_cells * rim[2, 2:, 1:-1],
        rim[1, :-2, 1:-1] * open_cells,
        cond_z * open_cells * ahead(open_cells, 2),
        base_shift + wall_term * wall,
    )
    rhs = source * open_cells
    levels = []
    fields = []
    sources = []
    residual = rhs
    for depth in range(LEVELS):
        group = 1
        if depth > 0:
            face_x, low_x, face_y, low_y, face_z, shift = faces
            faces = (
                coarse_face(face_x, 1, 1),
                coarse_face(low_x, 1, 0),
                coarse_face(face_y, 0, 1),
                coarse_face(low_y, 0, 0),
                coarse_face(face_z, 2, 1),
                0.25 * coarse_sum(shift),
            )
            rhs = 0.25 * coarse_sum(residual)
            if depth >= 2:
                group = 2 ** (depth - 1)
                stacked = jnp.stack((rhs,) + faces)
                partner = swapped(stacked, GY, depth - 2)
                upper = upper_flag(depth - 2) == 1
                folded = jnp.concatenate(
                    [jnp.where(upper, partner, stacked), jnp.where(upper, stacked, partner)], axis=1
                )
                rhs = folded[0]
                faces = tuple((folded[place] for place in range(1, 7)))
        level = assemble(faces, group)
        field = line_solve(level, rhs)
        if depth == LEVELS - 1:
            field = relax(level, field, rhs)
        else:
            residual = neighbour_terms(level, field)
        levels.append(level)
        fields.append(field)
        sources.append(rhs)
    correction = fields[-1]
    for depth in range(LEVELS - 2, -1, -1):
        if depth + 1 >= 2:
            half = correction.shape[0] // 2
            correction = lax.dynamic_slice_in_dim(correction, upper_flag(depth - 1) * half, half, 0)
        field = fields[depth] + prolong(correction)
        correction = relax(levels[depth], field, sources[depth])
    return correction


def solution(mesh):
    finer = Mesh(mesh.devices.reshape(mesh.shape["gx"], 8, 4, 2), ("gx", "gy_0", "gy_1", "gy_2"))
    return jax.shard_map(
        body,
        mesh=finer,
        in_specs=(
            P(GY, "gx", None),
            P(GY, "gx", None),
            P(GY, "gx", None),
            P(GY, "gx", None),
            P(GY, "gx", None),
        ),
        out_specs=P(GY, "gx", None),
        check_vma=False,
    )
```
